512 devices in a mesh: blk: 64 (over x, z, y_lo), rep: 8 (over y_hi, core).
Axes of the slice: x: 4, y: 8 (y_hi: 4, y_lo: 2; y = y_hi * 2 + y_lo), z: 8, core: 2. Of those that a mesh axis runs over, the one named last changes fastest.
Arguments:
- grad_out: bfloat16 [65536, 256], P(('blk', 'rep')), may hold values from -6 to 6
- preact: bfloat16 [65536, 256], P(('blk', 'rep')), may hold values from -6 to 6
- aggregated: bfloat16 [65536, 256], P(('blk', 'rep')), may hold values from -6 to 6
- weight: bfloat16 [256, 256], replicated, may hold values from -0.375 to 0.375
- degree: int32 [65536], P(('blk', 'rep')), may hold values from 4 to 64
- neighbors: int32 [64, 8, 64, 4, 8, 128], P('blk', 'rep'), may hold values from 0 to 127
- tile_col: int32 [64, 8, 64, 4], P('blk', 'rep'), may hold values from 0 to 7, as said below
- tile_count: int32 [64, 8, 64], P('blk', 'rep'), may hold values from 0 to 4, as said below
Outputs:
- grad_features: bfloat16 [65536, 256], P(('blk', 'rep'))
- grad_weight: float32 [256, 256], replicated
The draws below stay inside these ranges and needn't reach their ends.
Inputs may be any that keep to these rules, and one draw needn't show every extreme that they name: `tile_col`: the column tiles listed for one block, replica and source block are all different, also in slots at or past the count. `tile_count`: equal to 4 wherever the source block equals the block, and 0 wherever the source block is more than 2 blocks away from the block in both directions around the closed loop of 64 blocks.
All inputs are finite; a program needn't handle non-finite values.
Results may differ from the reference program's by a relative error of at most 0.0049.
Values may be sent and summed in bfloat16 or wider, within the bound.
No kernel may reach another device: no remote copies, remote signals or barrier semaphores. Data moves between devices by JAX's collectives and lax.ppermute only.
A program may use at most 64 MiB of HBM per device.

```python
import jax
import jax.numpy as jnp
from jax import lax

HID = 256
TILE = 128
K = 8
REACH = 2
CAP = 4
NODES = 65536
N_BLK = 64
N_REP = 8


def draw_tile_col(key, part):
    scores = jax.random.randint(jax.random.fold_in(key, 11), (N_BLK, N_REP, N_BLK, N_REP), 0, 65536)
    ranked = scores * N_REP + jnp.arange(N_REP, dtype=jnp.int32)
    ordering = jnp.argsort(ranked, axis=-1)
    return ordering[..., :CAP].astype(jnp.int32)


def draw_tile_count(key, part):
    ceiling = jax.random.randint(jax.random.fold_in(key, 21), (N_BLK, N_REP, 1), 1, CAP + 1)
    drawn = jax.random.randint(jax.random.fold_in(key, 22), (N_BLK, N_REP, N_BLK), 0, 1048576)
    counts = drawn % ceiling + 1
    block_ids = jnp.arange(N_BLK, dtype=jnp.int32)[:, None, None]
    source_ids = jnp.arange(N_BLK, dtype=jnp.int32)[None, None, :]
    upward = (source_ids - block_ids) % N_BLK
    downward = (block_ids - source_ids) % N_BLK
    nearby = jnp.logical_or(upward <= REACH, downward <= REACH)
    diagonal = block_ids == source_ids
    banded = jnp.where(nearby, counts, 0)
    return jnp.where(diagonal, CAP, banded).astype(jnp.int32)


def place_ends(values, stream_key, least, largest):
    index_at = [jax.random.randint(jax.random.fold_in(stream_key, axis), (), 0, length) for axis, length in enumerate(values.shape)]
    longest = values.shape.index(max(values.shape))
    next_to = index_at[:longest] + [(index_at[longest] + 1) % values.shape[longest]] + index_at[longest + 1:]
    return values.at[tuple(index_at)].set(least).at[tuple(next_to)].set(largest)


def steps_of(own_key, dims, split, smallest, high):
    level, own = 1.0, jax.random.fold_in(own_key, 6)
    for dim, blocks in split:
        draws = jnp.exp(jax.random.uniform(jax.random.fold_in(own, dim), (blocks,), jnp.float32, smallest / len(split), high / len(split)))
        level = level * jnp.repeat(draws, dims[dim] // blocks).reshape([-1 if axis == dim else 1 for axis in range(len(dims))])
    return level


def centred(own_key, dims, spread, reach, pieces=(), held_as=jnp.bfloat16):
    entries = spread * jax.random.normal(own_key, dims, jnp.float32)
    if pieces:
        entries = entries * steps_of(own_key, dims, pieces, -0.22, 0.18)
    return jnp.clip(entries, -reach, reach).astype(held_as)


def setup_inputs(seed: int = 0) -> dict:
    splits = jax.random.split(jax.random.key(seed), 9)
    grad_out = centred(splits[0], (NODES, HID), 1.0, 6.0, ((0, 512),))
    preact = centred(splits[1], (NODES, HID), 1.0, 6.0, ((0, 512),))
    aggregated = centred(splits[2], (NODES, HID), 1.0, 6.0, ((0, 512),))
    weight = centred(splits[3], (HID, HID), HID ** -0.5, 0.375)
    degree = place_ends(jax.random.randint(splits[4], (NODES,), 4, 65), jax.random.fold_in(splits[4], 1), 4, 64).astype(jnp.int32)
    neighbors = place_ends(jax.random.randint(splits[5], (N_BLK, N_REP, N_BLK, CAP, K, TILE), 0, TILE), jax.random.fold_in(splits[5], 1), 0, TILE - 1).astype(jnp.int32)
    tile_col = draw_tile_col(jax.random.fold_in(splits[8], 71), 0)
    tile_count = draw_tile_count(jax.random.fold_in(splits[8], 71), 0)
    return dict(grad_out=grad_out, preact=preact, aggregated=aggregated, weight=weight, degree=degree, neighbors=neighbors, tile_col=tile_col, tile_count=tile_count)


def reference(grad_out, preact, aggregated, weight, degree, neighbors, tile_col, tile_count):
    grad_pre = jnp.where(preact > 0, grad_out, jnp.zeros_like(grad_out))
    raw_weight = lax.dot_general(aggregated, grad_pre, (((0,), (0,)), ((), ())), preferred_element_type=jnp.float32)
    norm_value = jnp.sqrt(jnp.sum(raw_weight * raw_weight) + 1e-06)
    grad_weight = raw_weight * jnp.minimum(1.0, 128.0 / norm_value)
    inv_root = 1.0 / jnp.sqrt(degree.astype(jnp.float32))
    backward = lax.dot_general(grad_pre, weight, (((1,), (1,)), ((), ())), preferred_element_type=jnp.float32)
    scaled = (backward * inv_root[:, None]).astype(jnp.bfloat16)
    blocks_rows = scaled.reshape(N_BLK, N_REP, TILE, HID)
    positions = jnp.arange(TILE, dtype=jnp.int32)
    slot_index = jnp.arange(CAP, dtype=jnp.int32)
    replicas = jnp.arange(N_REP, dtype=jnp.int32)

    def one_device(block, replica):
        listed = neighbors[block, replica]
        adjacency = lax.optimization_barrier(jnp.sum((listed[:, :, :, None, :] == positions[None, None, None, :, None]).astype(jnp.float32), axis=2))
        present = (slot_index[None, :] < tile_count[block, replica][:, None]).astype(jnp.float32)
        adjacency = adjacency * present[:, :, None, None]
        row_data = lax.dynamic_index_in_dim(blocks_rows, replica, 1, keepdims=False).astype(jnp.float32)
        contribution = jnp.einsum('tsci,tif->tscf', adjacency, row_data)
        chooser = (tile_col[block, replica][:, :, None] == replicas[None, None, :]).astype(jnp.float32)
        return jnp.einsum('tsn,tscf->ncf', chooser, contribution)

    def one_block(block):

        def for_replica(replica):
            return one_device(block, replica)
        return lax.optimization_barrier(jnp.sum(lax.map(for_replica, replicas), axis=0))
    propagated = lax.map(one_block, jnp.arange(N_BLK, dtype=jnp.int32))
    propagated = propagated.reshape(NODES, HID)
    grad_features = (propagated * inv_root[:, None]).astype(jnp.bfloat16)
    return (grad_features, grad_weight)
```

```python
import jax
import jax.numpy as jnp
from jax import lax
from jax.sharding import PartitionSpec as P

REACH = 2


def fetched_from(x, axis, offset):
    size = lax.axis_size(axis)
    return lax.ppermute(x, axis, [(i, (i - offset) % size) for i in range(size)])


def on_device(grad_out, preact, aggregated, weight, degree, neighbors, tile_col, tile_count):
    grad_pre = jnp.where(preact > 0, grad_out, jnp.zeros_like(grad_out))
    local_weight = lax.dot_general(
        aggregated, grad_pre, (((0,), (0,)), ((), ())), preferred_element_type=jnp.float32
    )
    raw_weight = lax.psum(local_weight, ("blk", "rep"))
    norm_value = jnp.sqrt(jnp.sum(raw_weight * raw_weight) + 1e-06)
    grad_weight = raw_weight * jnp.minimum(1.0, 128.0 / norm_value)
    inv_root = 1.0 / jnp.sqrt(degree.astype(jnp.float32))
    backward = lax.dot_general(
        grad_pre, weight, (((1,), (1,)), ((), ())), preferred_element_type=jnp.float32
    )
    scaled = (backward * inv_root[:, None]).astype(jnp.bfloat16)

    blocks = lax.axis_size("blk")
    replicas = lax.axis_size("rep")
    own_block = lax.axis_index("blk")
    offsets = list(range(-REACH, REACH + 1))
    rows = jnp.stack(
        [scaled if d == 0 else fetched_from(scaled, "blk", d) for d in offsets]
    )
    sources = (own_block + jnp.array(offsets, jnp.int32)) % blocks
    listed = jnp.take(neighbors[0, 0], sources, axis=0)
    column_ids = jnp.take(tile_col[0, 0], sources, axis=0)
    present = jnp.take(tile_count[0, 0], sources, axis=0)
    slots_total = listed.shape[1]
    tile_side = listed.shape[3]
    hidden = scaled.shape[1]
    positions = jnp.arange(tile_side, dtype=jnp.int32)
    slot_index = jnp.arange(slots_total, dtype=jnp.int32)
    counts = jnp.sum(
        (listed[:, :, :, :, None] == positions[None, None, None, None, :]).astype(jnp.int32),
        axis=2,
    )
    chooser = jnp.logical_and(
        column_ids[:, :, None] == jnp.arange(replicas, dtype=jnp.int32)[None, None, :],
        (slot_index[None, :] < present[:, None])[:, :, None],
    ).astype(jnp.int32)
    merged = jnp.einsum("tsn,tsic->tinc", chooser, counts).astype(jnp.bfloat16)
    totals = jnp.einsum(
        "tinc,tif->ncf", merged, rows, preferred_element_type=jnp.float32
    )
    owned = lax.psum_scatter(totals, "rep", scatter_dimension=0, tiled=True)
    grad_features = (owned[0] * inv_root[:, None]).astype(jnp.bfloat16)
    return (grad_features, grad_weight)


def solution(mesh):
    return jax.shard_map(
        on_device,
        mesh=mesh,
        in_specs=(
            P(("blk", "rep"), None),
            P(("blk", "rep"), None),
            P(("blk", "rep"), None),
            P(),
            P(("blk", "rep")),
            P("blk", "rep", None, None, None, None),
            P("blk", "rep", None, None),
            P("blk", "rep", None),
        ),
        out_specs=(P(("blk", "rep"), None), P()),
        check_vma=False,
    )
```

```python
import jax
import jax.numpy as jnp
from jax import lax
from jax.sharding import PartitionSpec as P

REACH = 2


def fetched_from(x, axis, offset):
    size = lax.axis_size(axis)
    return lax.ppermute(x, axis, [(i, (i - offset) % size) for i in range(size)])


def summed_everywhere(x, axes, bits):
    size = 1
    for axis in axes:
        size *= lax.axis_size(axis)
    for bit in bits:
        x = x + lax.ppermute(x, axes, [(i, i ^ (1 << bit)) for i in range(size)])
    return x


def on_device(grad_out, preact, aggregated, weight, degree, neighbors, tile_col, tile_count):
    grad_pre = jnp.where(preact > 0, grad_out, jnp.zeros_like(grad_out))
    local_weight = lax.dot_general(
        aggregated, grad_pre, (((0,), (0,)), ((), ())), preferred_element_type=jnp.float32
    )
    raw_weight = summed_everywhere(local_weight, ("blk", "rep"), [0, 3, 4, 5, 6, 7, 8, 1, 2])
    norm_value = jnp.sqrt(jnp.sum(raw_weight * raw_weight) + 1e-06)
    grad_weight = raw_weight * jnp.minimum(1.0, 128.0 / norm_value)
    inv_root = 1.0 / jnp.sqrt(degree.astype(jnp.float32))
    backward = lax.dot_general(
        grad_pre, weight, (((1,), (1,)), ((), ())), preferred_element_type=jnp.float32
    )
    scaled = (backward * inv_root[:, None]).astype(jnp.bfloat16)

    blocks = lax.axis_size("blk")
    replicas = lax.axis_size("rep")
    own_block = lax.axis_index("blk")
    offsets = list(range(-REACH, REACH + 1))
    rows = jnp.stack(
        [scaled if d == 0 else fetched_from(scaled, "blk", d) for d in offsets]
    )
    sources = (own_block + jnp.array(offsets, jnp.int32)) % blocks
    listed = jnp.take(neighbors[0, 0], sources, axis=0)
    column_ids = jnp.take(tile_col[0, 0], sources, axis=0)
    present = jnp.take(tile_count[0, 0], sources, axis=0)
    slots_total = listed.shape[1]
    tile_side = listed.shape[3]
    hidden = scaled.shape[1]
    positions = jnp.arange(tile_side, dtype=jnp.int32)
    slot_index = jnp.arange(slots_total, dtype=jnp.int32)
    counts = jnp.sum(
        (listed[:, :, :, :, None] == positions[None, None, None, None, :]).astype(jnp.int32),
        axis=2,
    )
    chooser = jnp.logical_and(
        column_ids[:, :, None] == jnp.arange(replicas, dtype=jnp.int32)[None, None, :],
        (slot_index[None, :] < present[:, None])[:, :, None],
    ).astype(jnp.int32)
    merged = jnp.einsum("tsn,tsic->tinc", chooser, counts).astype(jnp.bfloat16)
    totals = jnp.einsum(
        "tinc,tif->ncf", merged, rows, preferred_element_type=jnp.float32
    )
    owned = lax.psum_scatter(totals, "rep", scatter_dimension=0, tiled=True)
    grad_features = (owned[0] * inv_root[:, None]).astype(jnp.bfloat16)
    return (grad_features, grad_weight)


def solution(mesh):
    return jax.shard_map(
        on_device,
        mesh=mesh,
        in_specs=(
            P(("blk", "rep"), None),
            P(("blk", "rep"), None),
            P(("blk", "rep"), None),
            P(),
            P(("blk", "rep")),
            P("blk", "rep", None, None, None, None),
            P("blk", "rep", None, None),
            P("blk", "rep", None),
        ),
        out_specs=(P(("blk", "rep"), None), P()),
        check_vma=False,
    )
```

```python
import jax
import jax.numpy as jnp
from jax import lax
from jax.sharding import PartitionSpec as P

REACH = 2


def fetched_from(x, axis, offset):
    size = lax.axis_size(axis)
    return lax.ppermute(x, axis, [(i, (i - offset) % size) for i in range(size)])


def summed_everywhere(x, axes, orders):
    size = 1
    for axis in axes:
        size *= lax.axis_size(axis)
    parts = jnp.split(x, len(orders), axis=0)
    for step in range(max(len(order) for order in orders)):
        parts = [
            part + lax.ppermute(part, axes, [(i, i ^ (1 << order[step])) for i in range(size)])
            if step < len(order)
            else part
            for part, order in zip(parts, orders)
        ]
    return jnp.concatenate(parts, axis=0)


def on_device(grad_out, preact, aggregated, weight, degree, neighbors, tile_col, tile_count):
    grad_pre = jnp.where(preact > 0, grad_out, jnp.zeros_like(grad_out))
    local_weight = lax.dot_general(
        aggregated, grad_pre, (((0,), (0,)), ((), ())), preferred_element_type=jnp.float32
    )
    paired = summed_everywhere(local_weight, ("blk", "rep"), [[0]])
    paired, grad_pre = lax.optimization_barrier((paired, grad_pre))
    raw_weight = summed_everywhere(
        paired, ("blk", "rep"), [[3, 4, 7, 1, 5, 8, 2, 6], [4, 7, 3, 5, 8, 1, 6, 2]]
    )
    norm_value = jnp.sqrt(jnp.sum(raw_weight * raw_weight) + 1e-06)
    grad_weight = raw_weight * jnp.minimum(1.0, 128.0 / norm_value)
    inv_root = 1.0 / jnp.sqrt(degree.astype(jnp.float32))
    backward = lax.dot_general(
        grad_pre, weight, (((1,), (1,)), ((), ())), preferred_element_type=jnp.float32
    )
    scaled = (backward * inv_root[:, None]).astype(jnp.bfloat16)

    blocks = lax.axis_size("blk")
    replicas = lax.axis_size("rep")
    own_block = lax.axis_index("blk")
    offsets = list(range(-REACH, REACH + 1))
    rows = jnp.stack(
        [scaled if d == 0 else fetched_from(scaled, "blk", d) for d in offsets]
    )
    sources = (own_block + jnp.array(offsets, jnp.int32)) % blocks
    listed = jnp.take(neighbors[0, 0], sources, axis=0)
    column_ids = jnp.take(tile_col[0, 0], sources, axis=0)
    present = jnp.take(tile_count[0, 0], sources, axis=0)
    slots_total = listed.shape[1]
    tile_side = listed.shape[3]
    hidden = scaled.shape[1]
    positions = jnp.arange(tile_side, dtype=jnp.int32)
    slot_index = jnp.arange(slots_total, dtype=jnp.int32)
    counts = jnp.sum(
        (listed[:, :, :, :, None] == positions[None, None, None, None, :]).astype(jnp.int32),
        axis=2,
    )
    chooser = jnp.logical_and(
        column_ids[:, :, None] == jnp.arange(replicas, dtype=jnp.int32)[None, None, :],
        (slot_index[None, :] < present[:, None])[:, :, None],
    ).astype(jnp.int32)
    merged = jnp.einsum("tsn,tsic->tinc", chooser, counts).astype(jnp.bfloat16)
    totals = jnp.einsum(
        "tinc,tif->ncf", merged, rows, preferred_element_type=jnp.float32
    )
    owned = lax.psum_scatter(totals, "rep", scatter_dimension=0, tiled=True)
    grad_features = (owned[0] * inv_root[:, None]).astype(jnp.bfloat16)
    return (grad_features, grad_weight)


def solution(mesh):
    return jax.shard_map(
        on_device,
        mesh=mesh,
        in_specs=(
            P(("blk", "rep"), None),
            P(("blk", "rep"), None),
            P(("blk", "rep"), None),
            P(),
            P(("blk", "rep")),
            P("blk", "rep", None, None, None, None),
            P("blk", "rep", None, None),
            P("blk", "rep", None),
        ),
        out_specs=(P(("blk", "rep"), None), P()),
        check_vma=False,
    )
```

```python
import jax
import jax.numpy as jnp
from jax import lax
from jax.sharding import PartitionSpec as P

REACH = 2


def fetched_from(x, axis, offset):
    size = lax.axis_size(axis)
    return lax.ppermute(x, axis, [(i, (i - offset) % size) for i in range(size)])


def summed_everywhere(x, axes, orders):
    size = 1
    for axis in axes:
        size *= lax.axis_size(axis)
    parts = jnp.split(x, len(orders), axis=0)
    for step in range(max(len(order) for order in orders)):
        parts = [
            part + lax.ppermute(part, axes, [(i, i ^ order[step]) for i in range(size)])
            if step < len(order)
            else part
            for part, order in zip(parts, orders)
        ]
    return jnp.concatenate(parts, axis=0)


def on_device(grad_out, preact, aggregated, weight, degree, neighbors, tile_col, tile_count):
    grad_pre = jnp.where(preact > 0, grad_out, jnp.zeros_like(grad_out))
    local_weight = lax.dot_general(
        aggregated, grad_pre, (((0,), (0,)), ((), ())), preferred_element_type=jnp.float32
    )
    y1, y2, y3 = 1 << 3, 1 << 1, (1 << 1) | (1 << 2) | (1 << 3)
    z1, z2, z3 = 1 << 4, 1 << 5, (1 << 4) | (1 << 5) | (1 << 6)
    x1, x2 = 1 << 7, (1 << 7) | (1 << 8)
    paired = summed_everywhere(local_weight, ("blk", "rep"), [[1]])
    paired, grad_pre = lax.optimization_barrier((paired, grad_pre))
    raw_weight = summed_everywhere(
        paired, ("blk", "rep"), [[y1, z1, x1, y2, z2, x2, y3, z3], [z1, x1, y1, z2, x2, y2, z3, y3]]
    )
    norm_value = jnp.sqrt(jnp.sum(raw_weight * raw_weight) + 1e-06)
    grad_weight = raw_weight * jnp.minimum(1.0, 128.0 / norm_value)
    inv_root = 1.0 / jnp.sqrt(degree.astype(jnp.float32))
    backward = lax.dot_general(
        grad_pre, weight, (((1,), (1,)), ((), ())), preferred_element_type=jnp.float32
    )
    scaled = (backward * inv_root[:, None]).astype(jnp.bfloat16)

    blocks = lax.axis_size("blk")
    replicas = lax.axis_size("rep")
    own_block = lax.axis_index("blk")
    offsets = list(range(-REACH, REACH + 1))
    rows = jnp.stack(
        [scaled if d == 0 else fetched_from(scaled, "blk", d) for d in offsets]
    )
    sources = (own_block + jnp.array(offsets, jnp.int32)) % blocks
    listed = jnp.take(neighbors[0, 0], sources, axis=0)
    column_ids = jnp.take(tile_col[0, 0], sources, axis=0)
    present = jnp.take(tile_count[0, 0], sources, axis=0)
    slots_total = listed.shape[1]
    tile_side = listed.shape[3]
    hidden = scaled.shape[1]
    positions = jnp.arange(tile_side, dtype=jnp.int32)
    slot_index = jnp.arange(slots_total, dtype=jnp.int32)
    counts = jnp.sum(
        (listed[:, :, :, :, None] == positions[None, None, None, None, :]).astype(jnp.int32),
        axis=2,
    )
    chooser = jnp.logical_and(
        column_ids[:, :, None] == jnp.arange(replicas, dtype=jnp.int32)[None, None, :],
        (slot_index[None, :] < present[:, None])[:, :, None],
    ).astype(jnp.int32)
    merged = jnp.einsum("tsn,tsic->tinc", chooser, counts).astype(jnp.bfloat16)
    totals = jnp.einsum(
        "tinc,tif->ncf", merged, rows, preferred_element_type=jnp.float32
    )
    owned = lax.psum_scatter(totals, "rep", scatter_dimension=0, tiled=True)
    grad_features = (owned[0] * inv_root[:, None]).astype(jnp.bfloat16)
    return (grad_features, grad_weight)


def solution(mesh):
    return jax.shard_map(
        on_device,
        mesh=mesh,
        in_specs=(
            P(("blk", "rep"), None),
            P(("blk", "rep"), None),
            P(("blk", "rep"), None),
            P(),
            P(("blk", "rep")),
            P("blk", "rep", None, None, None, None),
            P("blk", "rep", None, None),
            P("blk", "rep", None),
        ),
        out_specs=(P(("blk", "rep"), None), P()),
        check_vma=False,
    )
```

```python
import jax
import jax.numpy as jnp
from jax import lax
from jax.sharding import PartitionSpec as P

REACH = 2


def fetched_from(x, axis, offset):
    size = lax.axis_size(axis)
    return lax.ppermute(x, axis, [(i, (i - offset) % size) for i in range(size)])


def summed_everywhere(x, axes, orders):
    size = 1
    for axis in axes:
        size *= lax.axis_size(axis)
    parts = jnp.split(x, len(orders), axis=0)
    for step in range(max(len(order) for order in orders)):
        parts = [
            part + lax.ppermute(part, axes, [(i, i ^ order[step]) for i in range(size)])
            if step < len(order)
            else part
            for part, order in zip(parts, orders)
        ]
    return jnp.concatenate(parts, axis=0)


def on_device(grad_out, preact, aggregated, weight, degree, neighbors, tile_col, tile_count):
    grad_pre = jnp.where(preact > 0, grad_out, jnp.zeros_like(grad_out))
    local_weight = lax.dot_general(
        aggregated, grad_pre, (((0,), (0,)), ((), ())), preferred_element_type=jnp.float32
    )
    y1, y2, y3 = 1 << 3, 1 << 1, (1 << 1) | (1 << 2) | (1 << 3)
    z1, z2, z3 = 1 << 4, 1 << 5, (1 << 4) | (1 << 5) | (1 << 6)
    x1, x2 = 1 << 7, (1 << 7) | (1 << 8)
    paired = summed_everywhere(local_weight, ("blk", "rep"), [[1]])
    paired, grad_pre = lax.optimization_barrier((paired, grad_pre))
    early = summed_everywhere(paired, ("blk", "rep"), [[y1, z1, x1], [z1, x1, y1]])
    inv_root = 1.0 / jnp.sqrt(degree.astype(jnp.float32))
    backward = lax.dot_general(
        grad_pre, weight, (((1,), (1,)), ((), ())), preferred_element_type=jnp.float32
    )
    scaled = (backward * inv_root[:, None]).astype(jnp.bfloat16)
    early, scaled = lax.optimization_barrier((early, scaled))
    raw_weight = summed_everywhere(
        early, ("blk", "rep"), [[y2, z2, x2, y3, z3], [z2, x2, y2, z3, y3]]
    )
    norm_value = jnp.sqrt(jnp.sum(raw_weight * raw_weight) + 1e-06)
    grad_weight = raw_weight * jnp.minimum(1.0, 128.0 / norm_value)

    blocks = lax.axis_size("blk")
    replicas = lax.axis_size("rep")
    own_block = lax.axis_index("blk")
    offsets = list(range(-REACH, REACH + 1))
    rows = jnp.stack(
        [scaled if d == 0 else fetched_from(scaled, "blk", d) for d in offsets]
    )
    sources = (own_block + jnp.array(offsets, jnp.int32)) % blocks
    listed = jnp.take(neighbors[0, 0], sources, axis=0)
    column_ids = jnp.take(tile_col[0, 0], sources, axis=0)
    present = jnp.take(tile_count[0, 0], sources, axis=0)
    slots_total = listed.shape[1]
    tile_side = listed.shape[3]
    hidden = scaled.shape[1]
    positions = jnp.arange(tile_side, dtype=jnp.int32)
    slot_index = jnp.arange(slots_total, dtype=jnp.int32)
    counts = jnp.sum(
        (listed[:, :, :, :, None] == positions[None, None, None, None, :]).astype(jnp.int32),
        axis=2,
    )
    chooser = jnp.logical_and(
        column_ids[:, :, None] == jnp.arange(replicas, dtype=jnp.int32)[None, None, :],
        (slot_index[None, :] < present[:, None])[:, :, None],
    ).astype(jnp.int32)
    merged = jnp.einsum("tsn,tsic->tinc", chooser, counts).astype(jnp.bfloat16)
    totals = jnp.einsum(
        "tinc,tif->ncf", merged, rows, preferred_element_type=jnp.float32
    )
    owned = lax.psum_scatter(totals, "rep", scatter_dimension=0, tiled=True)
    grad_features = (owned[0] * inv_root[:, None]).astype(jnp.bfloat16)
    return (grad_features, grad_weight)


def solution(mesh):
    return jax.shard_map(
        on_device,
        mesh=mesh,
        in_specs=(
            P(("blk", "rep"), None),
            P(("blk", "rep"), None),
            P(("blk", "rep"), None),
            P(),
            P(("blk", "rep")),
            P("blk", "rep", None, None, None, None),
            P("blk", "rep", None, None),
            P("blk", "rep", None),
        ),
        out_specs=(P(("blk", "rep"), None), P()),
        check_vma=False,
    )
```

```python
import jax
import jax.numpy as jnp
from jax import lax
from jax.sharding import PartitionSpec as P

REACH = 2


def fetched_from(x, axis, offset):
    size = lax.axis_size(axis)
    return lax.ppermute(x, axis, [(i, (i - offset) % size) for i in range(size)])


def summed_everywhere(x, axes, orders):
    size = 1
    for axis in axes:
        size *= lax.axis_size(axis)
    parts = jnp.split(x, len(orders), axis=0)
    for step in range(max(len(order) for order in orders)):
        parts = [
            part + lax.ppermute(part, axes, [(i, i ^ order[step]) for i in range(size)])
            if step < len(order)
            else part
            for part, order in zip(parts, orders)
        ]
    return jnp.concatenate(parts, axis=0)


def on_device(grad_out, preact, aggregated, weight, degree, neighbors, tile_col, tile_count):
    grad_pre = jnp.where(preact > 0, grad_out, jnp.zeros_like(grad_out))
    local_weight = lax.dot_general(
        aggregated, grad_pre, (((0,), (0,)), ((), ())), preferred_element_type=jnp.float32
    )
    y1, y2, y3 = 1 << 3, 1 << 1, (1 << 1) | (1 << 2) | (1 << 3)
    z1, z2, z3 = 1 << 4, 1 << 5, (1 << 4) | (1 << 5) | (1 << 6)
    x1, x2 = 1 << 7, (1 << 7) | (1 << 8)
    devices = lax.axis_size("blk") * lax.axis_size("rep")
    core = lax.axis_index("rep") % 2
    rows_half = local_weight.shape[0] // 2
    lower, upper = local_weight[:rows_half], local_weight[rows_half:]
    kept = jnp.where(core == 0, lower, upper)
    given = jnp.where(core == 0, upper, lower)
    half = kept + lax.ppermute(given, ("blk", "rep"), [(i, i ^ 1) for i in range(devices)])
    half, grad_pre = lax.optimization_barrier((half, grad_pre))
    half = summed_everywhere(
        half, ("blk", "rep"), [[y1, z1, x1, y2, z2, x2, y3, z3], [z1, x1, y1, z2, x2, y2, z3, y3]]
    )
    other = lax.ppermute(half, ("blk", "rep"), [(i, i ^ 1) for i in range(devices)])
    raw_weight = jnp.where(
        core == 0, jnp.concatenate([half, other]), jnp.concatenate([other, half])
    )
    norm_value = jnp.sqrt(jnp.sum(raw_weight * raw_weight) + 1e-06)
    grad_weight = raw_weight * jnp.minimum(1.0, 128.0 / norm_value)
    inv_root = 1.0 / jnp.sqrt(degree.astype(jnp.float32))
    backward = lax.dot_general(
        grad_pre, weight, (((1,), (1,)), ((), ())), preferred_element_type=jnp.float32
    )
    scaled = (backward * inv_root[:, None]).astype(jnp.bfloat16)

    blocks = lax.axis_size("blk")
    replicas = lax.axis_size("rep")
    own_block = lax.axis_index("blk")
    offsets = list(range(-REACH, REACH + 1))
    rows = jnp.stack(
        [scaled if d == 0 else fetched_from(scaled, "blk", d) for d in offsets]
    )
    sources = (own_block + jnp.array(offsets, jnp.int32)) % blocks
    listed = jnp.take(neighbors[0, 0], sources, axis=0)
    column_ids = jnp.take(tile_col[0, 0], sources, axis=0)
    present = jnp.take(tile_count[0, 0], sources, axis=0)
    slots_total = listed.shape[1]
    tile_side = listed.shape[3]
    hidden = scaled.shape[1]
    positions = jnp.arange(tile_side, dtype=jnp.int32)
    slot_index = jnp.arange(slots_total, dtype=jnp.int32)
    counts = jnp.sum(
        (listed[:, :, :, :, None] == positions[None, None, None, None, :]).astype(jnp.int32),
        axis=2,
    )
    chooser = jnp.logical_and(
        column_ids[:, :, None] == jnp.arange(replicas, dtype=jnp.int32)[None, None, :],
        (slot_index[None, :] < present[:, None])[:, :, None],
    ).astype(jnp.int32)
    merged = jnp.einsum("tsn,tsic->tinc", chooser, counts).astype(jnp.bfloat16)
    totals = jnp.einsum(
        "tinc,tif->ncf", merged, rows, preferred_element_type=jnp.float32
    )
    owned = lax.psum_scatter(totals, "rep", scatter_dimension=0, tiled=True)
    grad_features = (owned[0] * inv_root[:, None]).astype(jnp.bfloat16)
    return (grad_features, grad_weight)


def solution(mesh):
    return jax.shard_map(
        on_device,
        mesh=mesh,
        in_specs=(
            P(("blk", "rep"), None),
            P(("blk", "rep"), None),
            P(("blk", "rep"), None),
            P(),
            P(("blk", "rep")),
            P("blk", "rep", None, None, None, None),
            P("blk", "rep", None, None),
            P("blk", "rep", None),
        ),
        out_specs=(P(("blk", "rep"), None), P()),
        check_vma=False,
    )
```

```python
import jax
import jax.numpy as jnp
from jax import lax
from jax.sharding import PartitionSpec as P

REACH = 2


def fetched_from(x, axis, offset):
    size = lax.axis_size(axis)
    return lax.ppermute(x, axis, [(i, (i - offset) % size) for i in range(size)])


def on_device(grad_out, preact, aggregated, weight, degree, neighbors, tile_col, tile_count):
    grad_pre = jnp.where(preact > 0, grad_out, jnp.zeros_like(grad_out))
    local_weight = lax.dot_general(
        aggregated, grad_pre, (((0,), (0,)), ((), ())), preferred_element_type=jnp.float32
    )
    inv_root = 1.0 / jnp.sqrt(degree.astype(jnp.float32))
    backward = lax.dot_general(
        grad_pre, weight, (((1,), (1,)), ((), ())), preferred_element_type=jnp.float32
    )
    scaled = (backward * inv_root[:, None]).astype(jnp.bfloat16)

    blocks = lax.axis_size("blk")
    replicas = lax.axis_size("rep")
    own_block = lax.axis_index("blk")
    offsets = list(range(-REACH, REACH + 1))
    rows = jnp.stack(
        [scaled if d == 0 else fetched_from(scaled, "blk", d) for d in offsets]
    )
    sources = (own_block + jnp.array(offsets, jnp.int32)) % blocks
    listed = jnp.take(neighbors[0, 0], sources, axis=0)
    column_ids = jnp.take(tile_col[0, 0], sources, axis=0)
    present = jnp.take(tile_count[0, 0], sources, axis=0)
    slots_total = listed.shape[1]
    tile_side = listed.shape[3]
    hidden = scaled.shape[1]
    positions = jnp.arange(tile_side, dtype=jnp.int32)
    slot_index = jnp.arange(slots_total, dtype=jnp.int32)
    counts = jnp.sum(
        (listed[:, :, :, :, None] == positions[None, None, None, None, :]).astype(jnp.int32),
        axis=2,
    )
    chooser = jnp.logical_and(
        column_ids[:, :, None] == jnp.arange(replicas, dtype=jnp.int32)[None, None, :],
        (slot_index[None, :] < present[:, None])[:, :, None],
    ).astype(jnp.int32)
    merged = jnp.einsum("tsn,tsic->tinc", chooser, counts).astype(jnp.bfloat16)
    totals = jnp.einsum(
        "tinc,tif->ncf", merged, rows, preferred_element_type=jnp.float32
    )
    owned = lax.psum_scatter(totals, "rep", scatter_dimension=0, tiled=True)
    local_weight, totals = lax.optimization_barrier((local_weight, totals))
    devices = lax.axis_size("blk") * lax.axis_size("rep")
    pieces = lax.all_to_all(
        local_weight.reshape(devices, -1), ("blk", "rep"), 0, 0, tiled=True
    )
    piece = jnp.sum(pieces, axis=0)
    raw_weight = lax.all_to_all(
        jnp.broadcast_to(piece, (devices,) + piece.shape), ("blk", "rep"), 0, 0, tiled=True
    ).reshape(local_weight.shape)
    norm_value = jnp.sqrt(jnp.sum(raw_weight * raw_weight) + 1e-06)
    grad_weight = raw_weight * jnp.minimum(1.0, 128.0 / norm_value)
    grad_features = (owned[0] * inv_root[:, None]).astype(jnp.bfloat16)
    return (grad_features, grad_weight)


def solution(mesh):
    return jax.shard_map(
        on_device,
        mesh=mesh,
        in_specs=(
            P(("blk", "rep"), None),
            P(("blk", "rep"), None),
            P(("blk", "rep"), None),
            P(),
            P(("blk", "rep")),
            P("blk", "rep", None, None, None, None),
            P("blk", "rep", None, None),
            P("blk", "rep", None),
        ),
        out_specs=(P(("blk", "rep"), None), P()),
        check_vma=False,
    )
```

```python
import jax
import jax.numpy as jnp
from jax import lax
from jax.sharding import PartitionSpec as P

REACH = 2


def fetched_from(x, axis, offset):
    size = lax.axis_size(axis)
    return lax.ppermute(x, axis, [(i, (i - offset) % size) for i in range(size)])


def on_device(grad_out, preact, aggregated, weight, degree, neighbors, tile_col, tile_count):
    grad_pre = jnp.where(preact > 0, grad_out, jnp.zeros_like(grad_out))
    local_weight = lax.dot_general(
        aggregated, grad_pre, (((0,), (0,)), ((), ())), preferred_element_type=jnp.float32
    )
    inv_root = 1.0 / jnp.sqrt(degree.astype(jnp.float32))
    backward = lax.dot_general(
        grad_pre, weight, (((1,), (1,)), ((), ())), preferred_element_type=jnp.float32
    )
    scaled = (backward * inv_root[:, None]).astype(jnp.bfloat16)

    blocks = lax.axis_size("blk")
    replicas = lax.axis_size("rep")
    own_block = lax.axis_index("blk")
    offsets = list(range(-REACH, REACH + 1))
    rows = jnp.stack(
        [scaled if d == 0 else fetched_from(scaled, "blk", d) for d in offsets]
    )
    sources = (own_block + jnp.array(offsets, jnp.int32)) % blocks
    listed = jnp.take(neighbors[0, 0], sources, axis=0)
    column_ids = jnp.take(tile_col[0, 0], sources, axis=0)
    present = jnp.take(tile_count[0, 0], sources, axis=0)
    slots_total = listed.shape[1]
    tile_side = listed.shape[3]
    hidden = scaled.shape[1]
    positions = jnp.arange(tile_side, dtype=jnp.int32)
    slot_index = jnp.arange(slots_total, dtype=jnp.int32)
    counts = jnp.sum(
        (listed[:, :, :, :, None] == positions[None, None, None, None, :]).astype(jnp.bfloat16),
        axis=2,
    )
    chooser = jnp.logical_and(
        column_ids[:, :, None] == jnp.arange(replicas, dtype=jnp.int32)[None, None, :],
        (slot_index[None, :] < present[:, None])[:, :, None],
    ).astype(jnp.bfloat16)
    merged = jnp.sum(
        chooser[:, :, None, :, None] * counts[:, :, :, None, :], axis=1
    )
    totals = jnp.einsum(
        "tinc,tif->ncf", merged, rows, preferred_element_type=jnp.float32
    )
    owned = lax.psum_scatter(totals, "rep", scatter_dimension=0, tiled=True)
    local_weight, totals = lax.optimization_barrier((local_weight, totals))
    devices = lax.axis_size("blk") * lax.axis_size("rep")
    pieces = lax.all_to_all(
        local_weight.reshape(devices, -1), ("blk", "rep"), 0, 0, tiled=True
    )
    piece = jnp.sum(pieces, axis=0)
    raw_weight = lax.all_to_all(
        jnp.broadcast_to(piece, (devices,) + piece.shape), ("blk", "rep"), 0, 0, tiled=True
    ).reshape(local_weight.shape)
    norm_value = jnp.sqrt(jnp.sum(raw_weight * raw_weight) + 1e-06)
    grad_weight = raw_weight * jnp.minimum(1.0, 128.0 / norm_value)
    grad_features = (owned[0] * inv_root[:, None]).astype(jnp.bfloat16)
    return (grad_features, grad_weight)


def solution(mesh):
    return jax.shard_map(
        on_device,
        mesh=mesh,
        in_specs=(
            P(("blk", "rep"), None),
            P(("blk", "rep"), None),
            P(("blk", "rep"), None),
            P(),
            P(("blk", "rep")),
            P("blk", "rep", None, None, None, None),
            P("blk", "rep", None, None),
            P("blk", "rep", None),
        ),
        out_specs=(P(("blk", "rep"), None), P()),
        check_vma=False,
    )
```

```python
import jax
import jax.numpy as jnp
from jax import lax
from jax.sharding import PartitionSpec as P

REACH = 2


def fetched_from(x, axis, offset):
    size = lax.axis_size(axis)
    return lax.ppermute(x, axis, [(i, (i - offset) % size) for i in range(size)])


def on_device(grad_out, preact, aggregated, weight, degree, neighbors, tile_col, tile_count):
    grad_pre = jnp.where(preact > 0, grad_out, jnp.zeros_like(grad_out))
    local_weight = lax.dot_general(
        aggregated, grad_pre, (((0,), (0,)), ((), ())), preferred_element_type=jnp.float32
    )
    inv_root = 1.0 / jnp.sqrt(degree.astype(jnp.float32))
    backward = lax.dot_general(
        grad_pre, weight, (((1,), (1,)), ((), ())), preferred_element_type=jnp.float32
    )
    scaled = (backward * inv_root[:, None]).astype(jnp.bfloat16)

    blocks = lax.axis_size("blk")
    replicas = lax.axis_size("rep")
    own_block = lax.axis_index("blk")
    offsets = list(range(-REACH, REACH + 1))
    sources = (own_block + jnp.array(offsets, jnp.int32)) % blocks
    listed = jnp.take(neighbors[0, 0], sources, axis=0)
    column_ids = jnp.take(tile_col[0, 0], sources, axis=0)
    present = jnp.take(tile_count[0, 0], sources, axis=0)
    slots_total = listed.shape[1]
    tile_side = listed.shape[3]
    hidden = scaled.shape[1]
    positions = jnp.arange(tile_side, dtype=jnp.int32)
    slot_index = jnp.arange(slots_total, dtype=jnp.int32)
    counts = jnp.sum(
        (listed[:, :, :, :, None] == positions[None, None, None, None, :]).astype(jnp.bfloat16),
        axis=2,
    )
    chooser = jnp.logical_and(
        column_ids[:, :, None] == jnp.arange(replicas, dtype=jnp.int32)[None, None, :],
        (slot_index[None, :] < present[:, None])[:, :, None],
    ).astype(jnp.bfloat16)
    merged = jnp.sum(
        chooser[:, :, None, :, None] * counts[:, :, :, None, :], axis=1
    )
    early = {d: fetched_from(scaled, "blk", d) for d in offsets if d < 0}
    later_source, merged = lax.optimization_barrier((scaled, merged))
    late = {d: fetched_from(later_source, "blk", d) for d in offsets if d > 0}
    rows = jnp.stack([scaled if d == 0 else {**early, **late}[d] for d in offsets])
    totals = jnp.einsum(
        "tinc,tif->ncf", merged, rows, preferred_element_type=jnp.float32
    )
    owned = lax.psum_scatter(totals, "rep", scatter_dimension=0, tiled=True)
    local_weight, totals = lax.optimization_barrier((local_weight, totals))
    devices = lax.axis_size("blk") * lax.axis_size("rep")
    pieces = lax.all_to_all(
        local_weight.reshape(devices, -1), ("blk", "rep"), 0, 0, tiled=True
    )
    piece = jnp.sum(pieces, axis=0)
    raw_weight = lax.all_to_all(
        jnp.broadcast_to(piece, (devices,) + piece.shape), ("blk", "rep"), 0, 0, tiled=True
    ).reshape(local_weight.shape)
    norm_value = jnp.sqrt(jnp.sum(raw_weight * raw_weight) + 1e-06)
    grad_weight = raw_weight * jnp.minimum(1.0, 128.0 / norm_value)
    grad_features = (owned[0] * inv_root[:, None]).astype(jnp.bfloat16)
    return (grad_features, grad_weight)


def solution(mesh):
    return jax.shard_map(
        on_device,
        mesh=mesh,
        in_specs=(
            P(("blk", "rep"), None),
            P(("blk", "rep"), None),
            P(("blk", "rep"), None),
            P(),
            P(("blk", "rep")),
            P("blk", "rep", None, None, None, None),
            P("blk", "rep", None, None),
            P("blk", "rep", None),
        ),
        out_specs=(P(("blk", "rep"), None), P()),
        check_vma=False,
    )
```

```python
import jax
import jax.numpy as jnp
from jax import lax
from jax.sharding import PartitionSpec as P

REACH = 2


def fetched_from(x, axis, offset):
    size = lax.axis_size(axis)
    return lax.ppermute(x, axis, [(i, (i - offset) % size) for i in range(size)])


def on_device(grad_out, preact, aggregated, weight, degree, neighbors, tile_col, tile_count):
    grad_pre = jnp.where(preact > 0, grad_out, jnp.zeros_like(grad_out))
    local_weight = lax.dot_general(
        aggregated, grad_pre, (((0,), (0,)), ((), ())), preferred_element_type=jnp.float32
    )
    inv_root = 1.0 / jnp.sqrt(degree.astype(jnp.float32))
    backward = lax.dot_general(
        grad_pre, weight, (((1,), (1,)), ((), ())), preferred_element_type=jnp.float32
    )
    scaled = (backward * inv_root[:, None]).astype(jnp.bfloat16)

    blocks = lax.axis_size("blk")
    replicas = lax.axis_size("rep")
    own_block = lax.axis_index("blk")
    offsets = list(range(-REACH, REACH + 1))
    rows = jnp.stack(
        [scaled if d == 0 else fetched_from(scaled, "blk", d) for d in offsets]
    )
    sources = (own_block + jnp.array(offsets, jnp.int32)) % blocks
    listed = jnp.take(neighbors[0, 0], sources, axis=0)
    column_ids = jnp.take(tile_col[0, 0], sources, axis=0)
    present = jnp.take(tile_count[0, 0], sources, axis=0)
    slots_total = listed.shape[1]
    tile_side = listed.shape[3]
    hidden = scaled.shape[1]
    positions = jnp.arange(tile_side, dtype=jnp.int32)
    slot_index = jnp.arange(slots_total, dtype=jnp.int32)
    counts = jnp.sum(
        (listed[:, :, :, :, None] == positions[None, None, None, None, :]).astype(jnp.int32),
        axis=2,
    )
    chooser = jnp.logical_and(
        column_ids[:, :, None] == jnp.arange(replicas, dtype=jnp.int32)[None, None, :],
        (slot_index[None, :] < present[:, None])[:, :, None],
    ).astype(jnp.int32)
    merged = jnp.einsum("tsn,tsic->tinc", chooser, counts).astype(jnp.bfloat16)
    totals = jnp.einsum(
        "tinc,tif->ncf", merged, rows, preferred_element_type=jnp.float32
    )
    rep_index = lax.axis_index("rep")

    def halved(parts, lower, upper, bit, mask):
        mine = (rep_index >> bit) & 1
        kept = jnp.where(mine == 0, lower, upper)
        given = jnp.where(mine == 0, upper, lower)
        return kept + lax.ppermute(given, "rep", [(i, i ^ mask) for i in range(replicas)])

    by_core = halved(totals, totals[0::2], totals[1::2], 0, 1)
    by_far = halved(by_core, by_core[:2], by_core[2:], 2, 6)
    owned = halved(by_far, by_far[0:1], by_far[1:2], 1, 2)
    local_weight, totals = lax.optimization_barrier((local_weight, totals))
    devices = lax.axis_size("blk") * lax.axis_size("rep")
    pieces = lax.all_to_all(
        local_weight.reshape(devices, -1), ("blk", "rep"), 0, 0, tiled=True
    )
    piece = jnp.sum(pieces, axis=0)
    raw_weight = lax.all_to_all(
        jnp.broadcast_to(piece, (devices,) + piece.shape), ("blk", "rep"), 0, 0, tiled=True
    ).reshape(local_weight.shape)
    norm_value = jnp.sqrt(jnp.sum(raw_weight * raw_weight) + 1e-06)
    grad_weight = raw_weight * jnp.minimum(1.0, 128.0 / norm_value)
    grad_features = (owned[0] * inv_root[:, None]).astype(jnp.bfloat16)
    return (grad_features, grad_weight)


def solution(mesh):
    return jax.shard_map(
        on_device,
        mesh=mesh,
        in_specs=(
            P(("blk", "rep"), None),
            P(("blk", "rep"), None),
            P(("blk", "rep"), None),
            P(),
            P(("blk", "rep")),
            P("blk", "rep", None, None, None, None),
            P("blk", "rep", None, None),
            P("blk", "rep", None),
        ),
        out_specs=(P(("blk", "rep"), None), P()),
        check_vma=False,
    )
```

```python
import jax
import jax.numpy as jnp
from jax import lax
from jax.sharding import PartitionSpec as P

REACH = 2


def fetched_from(x, axis, offset):
    size = lax.axis_size(axis)
    return lax.ppermute(x, axis, [(i, (i - offset) % size) for i in range(size)])


def on_device(grad_out, preact, aggregated, weight, degree, neighbors, tile_col, tile_count):
    grad_pre = jnp.where(preact > 0, grad_out, jnp.zeros_like(grad_out))
    local_weight = lax.dot_general(
        aggregated, grad_pre, (((0,), (0,)), ((), ())), preferred_element_type=jnp.float32
    )
    inv_root = 1.0 / jnp.sqrt(degree.astype(jnp.float32))
    backward = lax.dot_general(
        grad_pre, weight, (((1,), (1,)), ((), ())), preferred_element_type=jnp.float32
    )
    scaled = (backward * inv_root[:, None]).astype(jnp.bfloat16)

    blocks = lax.axis_size("blk")
    replicas = lax.axis_size("rep")
    own_block = lax.axis_index("blk")
    offsets = list(range(-REACH, REACH + 1))
    rows = jnp.stack(
        [scaled if d == 0 else fetched_from(scaled, "blk", d) for d in offsets]
    )
    sources = (own_block + jnp.array(offsets, jnp.int32)) % blocks
    listed = jnp.take(neighbors[0, 0], sources, axis=0)
    column_ids = jnp.take(tile_col[0, 0], sources, axis=0)
    present = jnp.take(tile_count[0, 0], sources, axis=0)
    slots_total = listed.shape[1]
    tile_side = listed.shape[3]
    hidden = scaled.shape[1]
    positions = jnp.arange(tile_side, dtype=jnp.int32)
    slot_index = jnp.arange(slots_total, dtype=jnp.int32)
    counts = jnp.sum(
        (listed[:, :, :, :, None] == positions[None, None, None, None, :]).astype(jnp.bfloat16),
        axis=2,
    )
    chooser = jnp.logical_and(
        column_ids[:, :, None] == jnp.arange(replicas, dtype=jnp.int32)[None, None, :],
        (slot_index[None, :] < present[:, None])[:, :, None],
    ).astype(jnp.bfloat16)
    merged = jnp.sum(
        chooser[:, :, None, :, None] * counts[:, :, :, None, :], axis=1
    )
    totals = jnp.einsum(
        "tinc,tif->ncf", merged, rows, preferred_element_type=jnp.float32
    )
    rep_index = lax.axis_index("rep")

    def halved(parts, lower, upper, bit, mask):
        mine = (rep_index >> bit) & 1
        kept = jnp.where(mine == 0, lower, upper)
        given = jnp.where(mine == 0, upper, lower)
        return kept + lax.ppermute(given, "rep", [(i, i ^ mask) for i in range(replicas)])

    by_core = halved(totals, totals[0::2], totals[1::2], 0, 1)
    by_far = halved(by_core, by_core[:2], by_core[2:], 2, 6)
    owned = halved(by_far, by_far[0:1], by_far[1:2], 1, 2)
    local_weight, totals = lax.optimization_barrier((local_weight, totals))
    devices = lax.axis_size("blk") * lax.axis_size("rep")
    pieces = lax.all_to_all(
        local_weight.reshape(devices, -1), ("blk", "rep"), 0, 0, tiled=True
    )
    piece = jnp.sum(pieces, axis=0)
    raw_weight = lax.all_to_all(
        jnp.broadcast_to(piece, (devices,) + piece.shape), ("blk", "rep"), 0, 0, tiled=True
    ).reshape(local_weight.shape)
    norm_value = jnp.sqrt(jnp.sum(raw_weight * raw_weight) + 1e-06)
    grad_weight = raw_weight * jnp.minimum(1.0, 128.0 / norm_value)
    grad_features = (owned[0] * inv_root[:, None]).astype(jnp.bfloat16)
    return (grad_features, grad_weight)


def solution(mesh):
    return jax.shard_map(
        on_device,
        mesh=mesh,
        in_specs=(
            P(("blk", "rep"), None),
            P(("blk", "rep"), None),
            P(("blk", "rep"), None),
            P(),
            P(("blk", "rep")),
            P("blk", "rep", None, None, None, None),
            P("blk", "rep", None, None),
            P("blk", "rep", None),
        ),
        out_specs=(P(("blk", "rep"), None), P()),
        check_vma=False,
    )
```

```python
import jax
import jax.numpy as jnp
from jax import lax
from jax.sharding import PartitionSpec as P

REACH = 2


def fetched_from(x, axis, offset):
    size = lax.axis_size(axis)
    return lax.ppermute(x, axis, [(i, (i - offset) % size) for i in range(size)])


def on_device(grad_out, preact, aggregated, weight, degree, neighbors, tile_col, tile_count):
    grad_pre = jnp.where(preact > 0, grad_out, jnp.zeros_like(grad_out))
    local_weight = lax.dot_general(
        aggregated, grad_pre, (((0,), (0,)), ((), ())), preferred_element_type=jnp.float32
    )
    inv_root = 1.0 / jnp.sqrt(degree.astype(jnp.float32))
    backward = lax.dot_general(
        grad_pre, weight, (((1,), (1,)), ((), ())), preferred_element_type=jnp.float32
    )
    scaled = (backward * inv_root[:, None]).astype(jnp.bfloat16)

    blocks = lax.axis_size("blk")
    replicas = lax.axis_size("rep")
    own_block = lax.axis_index("blk")
    offsets = list(range(-REACH, REACH + 1))
    rows = jnp.stack(
        [scaled if d == 0 else fetched_from(scaled, "blk", d) for d in offsets]
    )
    sources = (own_block + jnp.array(offsets, jnp.int32)) % blocks
    listed = jnp.take(neighbors[0, 0], sources, axis=0)
    column_ids = jnp.take(tile_col[0, 0], sources, axis=0)
    present = jnp.take(tile_count[0, 0], sources, axis=0)
    slots_total = listed.shape[1]
    tile_side = listed.shape[3]
    hidden = scaled.shape[1]
    positions = jnp.arange(tile_side, dtype=jnp.int32)
    slot_index = jnp.arange(slots_total, dtype=jnp.int32)
    counts = jnp.sum(
        (listed[:, :, :, :, None] == positions[None, None, None, None, :]).astype(jnp.bfloat16),
        axis=2,
    )
    chooser = jnp.logical_and(
        column_ids[:, :, None] == jnp.arange(replicas, dtype=jnp.int32)[None, None, :],
        (slot_index[None, :] < present[:, None])[:, :, None],
    ).astype(jnp.bfloat16)
    merged = jnp.sum(
        chooser[:, :, None, :, None] * counts[:, :, :, None, :], axis=1
    )
    totals = jnp.einsum(
        "tinc,tif->ncf", merged, rows, preferred_element_type=jnp.float32
    )
    rep_index = lax.axis_index("rep")

    def halved(parts, lower, upper, bit, mask):
        mine = (rep_index >> bit) & 1
        kept = jnp.where(mine == 0, lower, upper)
        given = jnp.where(mine == 0, upper, lower)
        return kept + lax.ppermute(given, "rep", [(i, i ^ mask) for i in range(replicas)])

    by_core = halved(totals, totals[0::2], totals[1::2], 0, 1)
    by_far = halved(by_core, by_core[:2], by_core[2:], 2, 6)
    owned = halved(by_far, by_far[0:1], by_far[1:2], 1, 2)
    devices = lax.axis_size("blk") * lax.axis_size("rep")
    pieces = lax.all_to_all(
        local_weight.reshape(devices, -1), ("blk", "rep"), 0, 0, tiled=True
    )
    piece = jnp.sum(pieces, axis=0)
    raw_weight = lax.all_to_all(
        jnp.broadcast_to(piece, (devices,) + piece.shape), ("blk", "rep"), 0, 0, tiled=True
    ).reshape(local_weight.shape)
    norm_value = jnp.sqrt(jnp.sum(raw_weight * raw_weight) + 1e-06)
    grad_weight = raw_weight * jnp.minimum(1.0, 128.0 / norm_value)
    grad_features = (owned[0] * inv_root[:, None]).astype(jnp.bfloat16)
    return (grad_features, grad_weight)


def solution(mesh):
    return jax.shard_map(
        on_device,
        mesh=mesh,
        in_specs=(
            P(("blk", "rep"), None),
            P(("blk", "rep"), None),
            P(("blk", "rep"), None),
            P(),
            P(("blk", "rep")),
            P("blk", "rep", None, None, None, None),
            P("blk", "rep", None, None),
            P("blk", "rep", None),
        ),
        out_specs=(P(("blk", "rep"), None), P()),
        check_vma=False,
    )
```

```python
import jax
import jax.numpy as jnp
from jax import lax
from jax.sharding import PartitionSpec as P

REACH = 2


def fetched_from(x, axis, offset):
    size = lax.axis_size(axis)
    return lax.ppermute(x, axis, [(i, (i - offset) % size) for i in range(size)])


def on_device(grad_out, preact, aggregated, weight, degree, neighbors, tile_col, tile_count):
    grad_pre = jnp.where(preact > 0, grad_out, jnp.zeros_like(grad_out))
    local_weight = lax.dot_general(
        aggregated, grad_pre, (((0,), (0,)), ((), ())), preferred_element_type=jnp.float32
    )
    inv_root = 1.0 / jnp.sqrt(degree.astype(jnp.float32))
    backward = lax.dot_general(
        grad_pre, weight, (((1,), (1,)), ((), ())), preferred_element_type=jnp.float32
    )
    scaled = (backward * inv_root[:, None]).astype(jnp.bfloat16)
    devices = lax.axis_size("blk") * lax.axis_size("rep")
    pieces = lax.all_to_all(
        local_weight.reshape(devices, -1), ("blk", "rep"), 0, 0, tiled=True
    )
    scaled, pieces = lax.optimization_barrier((scaled, pieces))

    blocks = lax.axis_size("blk")
    replicas = lax.axis_size("rep")
    own_block = lax.axis_index("blk")
    offsets = list(range(-REACH, REACH + 1))
    rows = jnp.stack(
        [scaled if d == 0 else fetched_from(scaled, "blk", d) for d in offsets]
    )
    sources = (own_block + jnp.array(offsets, jnp.int32)) % blocks
    listed = jnp.take(neighbors[0, 0], sources, axis=0)
    column_ids = jnp.take(tile_col[0, 0], sources, axis=0)
    present = jnp.take(tile_count[0, 0], sources, axis=0)
    slots_total = listed.shape[1]
    tile_side = listed.shape[3]
    hidden = scaled.shape[1]
    positions = jnp.arange(tile_side, dtype=jnp.int32)
    slot_index = jnp.arange(slots_total, dtype=jnp.int32)
    counts = jnp.sum(
        (listed[:, :, :, :, None] == positions[None, None, None, None, :]).astype(jnp.bfloat16),
        axis=2,
    )
    chooser = jnp.logical_and(
        column_ids[:, :, None] == jnp.arange(replicas, dtype=jnp.int32)[None, None, :],
        (slot_index[None, :] < present[:, None])[:, :, None],
    ).astype(jnp.bfloat16)
    merged = jnp.sum(
        chooser[:, :, None, :, None] * counts[:, :, :, None, :], axis=1
    )
    totals = jnp.einsum(
        "tinc,tif->ncf", merged, rows, preferred_element_type=jnp.float32
    )
    rep_index = lax.axis_index("rep")

    def halved(parts, lower, upper, bit, mask):
        mine = (rep_index >> bit) & 1
        kept = jnp.where(mine == 0, lower, upper)
        given = jnp.where(mine == 0, upper, lower)
        return kept + lax.ppermute(given, "rep", [(i, i ^ mask) for i in range(replicas)])

    by_core = halved(totals, totals[0::2], totals[1::2], 0, 1)
    by_far = halved(by_core, by_core[:2], by_core[2:], 2, 6)
    owned = halved(by_far, by_far[0:1], by_far[1:2], 1, 2)
    piece, totals = lax.optimization_barrier((jnp.sum(pieces, axis=0), totals))
    raw_weight = lax.all_to_all(
        jnp.broadcast_to(piece, (devices,) + piece.shape), ("blk", "rep"), 0, 0, tiled=True
    ).reshape(local_weight.shape)
    norm_value = jnp.sqrt(jnp.sum(raw_weight * raw_weight) + 1e-06)
    grad_weight = raw_weight * jnp.minimum(1.0, 128.0 / norm_value)
    grad_features = (owned[0] * inv_root[:, None]).astype(jnp.bfloat16)
    return (grad_features, grad_weight)


def solution(mesh):
    return jax.shard_map(
        on_device,
        mesh=mesh,
        in_specs=(
            P(("blk", "rep"), None),
            P(("blk", "rep"), None),
            P(("blk", "rep"), None),
            P(),
            P(("blk", "rep")),
            P("blk", "rep", None, None, None, None),
            P("blk", "rep", None, None),
            P("blk", "rep", None),
        ),
        out_specs=(P(("blk", "rep"), None), P()),
        check_vma=False,
    )
```

```python
import jax
import jax.numpy as jnp
from jax import lax
from jax.sharding import PartitionSpec as P

REACH = 2


def fetched_from(x, axis, offset):
    size = lax.axis_size(axis)
    return lax.ppermute(x, axis, [(i, (i - offset) % size) for i in range(size)])


def on_device(grad_out, preact, aggregated, weight, degree, neighbors, tile_col, tile_count):
    grad_pre = jnp.where(preact > 0, grad_out, jnp.zeros_like(grad_out))
    local_weight = lax.dot_general(
        aggregated, grad_pre, (((0,), (0,)), ((), ())), preferred_element_type=jnp.float32
    )
    inv_root = 1.0 / jnp.sqrt(degree.astype(jnp.float32))
    backward = lax.dot_general(
        grad_pre, weight, (((1,), (1,)), ((), ())), preferred_element_type=jnp.float32
    )
    scaled = (backward * inv_root[:, None]).astype(jnp.bfloat16)

    blocks = lax.axis_size("blk")
    replicas = lax.axis_size("rep")
    own_block = lax.axis_index("blk")
    offsets = list(range(-REACH, REACH + 1))
    rows = jnp.stack(
        [scaled if d == 0 else fetched_from(scaled, "blk", d) for d in offsets]
    )
    sources = (own_block + jnp.array(offsets, jnp.int32)) % blocks
    listed = jnp.take(neighbors[0, 0], sources, axis=0)
    column_ids = jnp.take(tile_col[0, 0], sources, axis=0)
    present = jnp.take(tile_count[0, 0], sources, axis=0)
    slots_total = listed.shape[1]
    tile_side = listed.shape[3]
    hidden = scaled.shape[1]
    positions = jnp.arange(tile_side, dtype=jnp.int32)
    slot_index = jnp.arange(slots_total, dtype=jnp.int32)
    counts = jnp.sum(
        (listed[:, :, :, :, None] == positions[None, None, None, None, :]).astype(jnp.bfloat16),
        axis=2,
    )
    chooser = jnp.logical_and(
        column_ids[:, :, None] == jnp.arange(replicas, dtype=jnp.int32)[None, None, :],
        (slot_index[None, :] < present[:, None])[:, :, None],
    ).astype(jnp.bfloat16)
    merged = jnp.sum(
        chooser[:, :, None, :, None] * counts[:, :, :, None, :], axis=1
    )
    totals = jnp.einsum(
        "tinc,tif->ncf", merged, rows, preferred_element_type=jnp.float32
    )
    rep_index = lax.axis_index("rep")

    def halved(parts, lower, upper, bit, mask):
        mine = (rep_index >> bit) & 1
        kept = jnp.where(mine == 0, lower, upper)
        given = jnp.where(mine == 0, upper, lower)
        return kept + lax.ppermute(given, "rep", [(i, i ^ mask) for i in range(replicas)])

    by_core = halved(totals, totals[0::2], totals[1::2], 0, 1)
    by_far = halved(by_core, by_core[:2], by_core[2:], 2, 6)
    owned = halved(by_far, by_far[0:1], by_far[1:2], 1, 2)
    local_weight, totals = lax.optimization_barrier((local_weight, totals))
    devices = lax.axis_size("blk") * lax.axis_size("rep")
    pieces = lax.all_to_all(
        local_weight.reshape(devices, -1), ("blk", "rep"), 0, 0, tiled=True
    )
    piece = jnp.sum(pieces, axis=0)
    squares = jnp.zeros_like(piece).at[0].set(jnp.sum(piece * piece))
    sent = jnp.stack([piece, squares])
    gathered = lax.all_to_all(
        jnp.broadcast_to(sent, (devices,) + sent.shape), ("blk", "rep"), 0, 0, tiled=True
    )
    raw_weight = gathered[:, 0].reshape(local_weight.shape)
    norm_value = jnp.sqrt(jnp.sum(gathered[:, 1, 0]) + 1e-06)
    grad_weight = raw_weight * jnp.minimum(1.0, 128.0 / norm_value)
    grad_features = (owned[0] * inv_root[:, None]).astype(jnp.bfloat16)
    return (grad_features, grad_weight)


def solution(mesh):
    return jax.shard_map(
        on_device,
        mesh=mesh,
        in_specs=(
            P(("blk", "rep"), None),
            P(("blk", "rep"), None),
            P(("blk", "rep"), None),
            P(),
            P(("blk", "rep")),
            P("blk", "rep", None, None, None, None),
            P("blk", "rep", None, None),
            P("blk", "rep", None),
        ),
        out_specs=(P(("blk", "rep"), None), P()),
        check_vma=False,
    )
```

```python
import jax
import jax.numpy as jnp
from jax import lax
from jax.sharding import PartitionSpec as P

REACH = 2


def fetched_from(x, axis, offset):
    size = lax.axis_size(axis)
    return lax.ppermute(x, axis, [(i, (i - offset) % size) for i in range(size)])


def on_device(grad_out, preact, aggregated, weight, degree, neighbors, tile_col, tile_count):
    grad_pre = jnp.where(preact > 0, grad_out, jnp.zeros_like(grad_out))
    local_weight = lax.dot_general(
        aggregated, grad_pre, (((0,), (0,)), ((), ())), preferred_element_type=jnp.float32
    )
    inv_root = 1.0 / jnp.sqrt(degree.astype(jnp.float32))
    backward = lax.dot_general(
        grad_pre, weight, (((1,), (1,)), ((), ())), preferred_element_type=jnp.float32
    )
    scaled = (backward * inv_root[:, None]).astype(jnp.bfloat16)

    blocks = lax.axis_size("blk")
    replicas = lax.axis_size("rep")
    own_block = lax.axis_index("blk")
    offsets = list(range(-REACH, REACH + 1))
    rows = jnp.stack(
        [scaled if d == 0 else fetched_from(scaled, "blk", d) for d in offsets]
    )
    sources = (own_block + jnp.array(offsets, jnp.int32)) % blocks
    listed = jnp.take(neighbors[0, 0], sources, axis=0)
    slot_table = jnp.take(
        jnp.concatenate([tile_col[0, 0], tile_count[0, 0][:, None]], axis=1), sources, axis=0
    )
    column_ids, present = slot_table[:, :-1], slot_table[:, -1]
    slots_total = listed.shape[1]
    tile_side = listed.shape[3]
    hidden = scaled.shape[1]
    positions = jnp.arange(tile_side, dtype=jnp.int32)
    slot_index = jnp.arange(slots_total, dtype=jnp.int32)
    counts = jnp.sum(
        (listed[:, :, :, :, None] == positions[None, None, None, None, :]).astype(jnp.bfloat16),
        axis=2,
    )
    chooser = jnp.logical_and(
        column_ids[:, :, None] == jnp.arange(replicas, dtype=jnp.int32)[None, None, :],
        (slot_index[None, :] < present[:, None])[:, :, None],
    ).astype(jnp.bfloat16)
    merged = jnp.sum(
        chooser[:, :, None, :, None] * counts[:, :, :, None, :], axis=1
    )
    totals = jnp.einsum(
        "tinc,tif->ncf", merged, rows, preferred_element_type=jnp.float32
    )
    rep_index = lax.axis_index("rep")

    def halved(parts, lower, upper, bit, mask):
        mine = (rep_index >> bit) & 1
        kept = jnp.where(mine == 0, lower, upper)
        given = jnp.where(mine == 0, upper, lower)
        return kept + lax.ppermute(given, "rep", [(i, i ^ mask) for i in range(replicas)])

    by_core = halved(totals, totals[0::2], totals[1::2], 0, 1)
    by_far = halved(by_core, by_core[:2], by_core[2:], 2, 6)
    owned = halved(by_far, by_far[0:1], by_far[1:2], 1, 2)
    local_weight, totals = lax.optimization_barrier((local_weight, totals))
    devices = lax.axis_size("blk") * lax.axis_size("rep")
    pieces = lax.all_to_all(
        local_weight.reshape(devices, -1), ("blk", "rep"), 0, 0, tiled=True
    )
    piece = jnp.sum(pieces, axis=0)
    raw_weight = lax.all_to_all(
        jnp.broadcast_to(piece, (devices,) + piece.shape), ("blk", "rep"), 0, 0, tiled=True
    ).reshape(local_weight.shape)
    norm_value = jnp.sqrt(jnp.sum(raw_weight * raw_weight) + 1e-06)
    grad_weight = raw_weight * jnp.minimum(1.0, 128.0 / norm_value)
    grad_features = (owned[0] * inv_root[:, None]).astype(jnp.bfloat16)
    return (grad_features, grad_weight)


def solution(mesh):
    return jax.shard_map(
        on_device,
        mesh=mesh,
        in_specs=(
            P(("blk", "rep"), None),
            P(("blk", "rep"), None),
            P(("blk", "rep"), None),
            P(),
            P(("blk", "rep")),
            P("blk", "rep", None, None, None, None),
            P("blk", "rep", None, None),
            P("blk", "rep", None),
        ),
        out_specs=(P(("blk", "rep"), None), P()),
        check_vma=False,
    )
```
